768 devices in a mesh: segment: 8 (over x, core), field: 12 (over z), row: 8 (over y).
Axes of the slice: x: 4, y: 8, z: 12, core: 2. Of those that a mesh axis runs over, the one named last changes fastest.
Arguments:
- embeddings: bfloat16 [8, 1024, 192, 256], P('segment', 'row', 'field'), may hold values from -6 to 6
- compress: bfloat16 [8, 192, 8], P('segment'), may hold values from -1.5 to 1.5
- mixing: bfloat16 [8, 1536, 49152], P('segment', None, ('field', 'row')), may hold values from -0.15625 to 0.15625
- rescale_factor: float32 [8, 192, 256], P('segment', 'field'), may hold values from 0.5 to 1.5
- active_block_flags: int32 [12, 3], P('field'), may hold values from 1 to 3
Outputs:
- handed_on: bfloat16 [8, 1024, 192, 256], P('segment', 'row', 'field')
The draws below stay inside these ranges and needn't reach their ends.
All inputs are finite; a program needn't handle non-finite values.
Results may differ from the reference program's by a relative error of at most 0.013.
Values may be sent and summed in bfloat16 or wider, within the bound.
No kernel may reach another device: no remote copies, remote signals or barrier semaphores. Data moves between devices by JAX's collectives and lax.ppermute only.
A program may use at most 128 MiB of HBM per device.

```python
import math
import jax
import jax.numpy as jnp
from jax import lax

E = 256
FIELD_DEV = 16
RANK = 8
ROWS = 1024
FEATURE_COUNT = 192
RELAY_SECTIONS = 8
N_FIELD = 12


def plant(values, rng, low, top_value):
    index_at = [jax.random.randint(jax.random.fold_in(rng, axis), (), 0, length) for axis, length in enumerate(values.shape)]
    main_axis = values.shape.index(max(values.shape))
    neighbour = index_at[:main_axis] + [(index_at[main_axis] + 1) % values.shape[main_axis]] + index_at[main_axis + 1:]
    return values.at[tuple(index_at)].set(low).at[tuple(neighbour)].set(top_value)


def steps_of(rng, dims, shards, least, largest):
    level = 1.0
    for axis_at, blocks in shards:
        draws = jax.random.uniform(jax.random.fold_in(jax.random.fold_in(rng, 6), axis_at), (blocks,), jnp.float32, least / len(shards), largest / len(shards))
        level = level * jnp.repeat(jnp.exp(draws), dims[axis_at] // blocks).reshape((-1,) + (1,) * (len(dims) - 1 - axis_at))
    return level


def normal_values(key, dims, width, most, pieces=(), dtype=jnp.bfloat16):
    drawn = jax.random.normal(key, dims, jnp.float32) * width
    if len(pieces) > 0:
        drawn = steps_of(key, dims, pieces, -0.22, 0.18) * drawn
    return jnp.clip(drawn, min=-most, max=most).astype(dtype)


def setup_inputs(seed: int = 0) -> dict:
    key_of = jax.random.split(jax.random.key(seed), 6)
    return {
        "embeddings": normal_values(key_of[0], (RELAY_SECTIONS, ROWS, FEATURE_COUNT, E), 1.0, 6.0, ((0, 8), (1, 8), (2, 12))),
        "compress": normal_values(key_of[1], (RELAY_SECTIONS, FEATURE_COUNT, RANK), FIELD_DEV ** -0.5, 1.5, ((0, 8),)),
        "mixing": normal_values(key_of[2], (RELAY_SECTIONS, FEATURE_COUNT * RANK, FEATURE_COUNT * E), (FEATURE_COUNT * RANK) ** -0.5, 0.15625, ((0, 8), (2, 96))),
        "rescale_factor": jnp.clip(1.0 + 0.1 * jax.random.normal(key_of[3], (RELAY_SECTIONS, FEATURE_COUNT, E), jnp.float32), 0.5, 1.5),
        "active_block_flags": plant(jax.random.randint(key_of[4], (N_FIELD, 3), 1, 4), jax.random.fold_in(key_of[4], 1), 1, 3).astype(jnp.int32),
    }


def one_section(section_panels, section_compress, section_mixing, section_gain, active_block_flags):
    shaped = section_panels.reshape(ROWS, N_FIELD, FIELD_DEV, E).astype(jnp.float32)
    compress_f = section_compress.reshape(N_FIELD, FIELD_DEV, RANK).astype(jnp.float32)
    reduced = jnp.einsum('bak,rbae->rbke', compress_f, shaped).astype(jnp.bfloat16)
    reduced = lax.optimization_barrier(reduced).astype(jnp.float32)
    block_activity = active_block_flags.astype(jnp.float32)
    pairwise_feature_product = jnp.zeros((ROWS, N_FIELD, FIELD_DEV, RANK), jnp.float32)
    for offset_ordinal in range(3):
        partner = jnp.roll(reduced, 1 - offset_ordinal, axis=1)
        lone_block_product = jnp.einsum('rbae,rbke->rbak', shaped, partner)
        pairwise_feature_product = pairwise_feature_product + block_activity[:, offset_ordinal][None, :, None, None] * lone_block_product
    scaled = (pairwise_feature_product * (1.0 / math.sqrt(E))).astype(jnp.bfloat16).reshape(ROWS, FEATURE_COUNT * RANK)
    mixed = jnp.dot(scaled, section_mixing, preferred_element_type=jnp.float32).astype(jnp.bfloat16)
    mixed = lax.optimization_barrier(mixed).astype(jnp.float32).reshape(ROWS, FEATURE_COUNT, E)
    summed = section_panels.astype(jnp.float32) + mixed
    mean_square = lax.optimization_barrier(jnp.mean(summed * summed, axis=-1, keepdims=True))
    return (summed * lax.rsqrt(mean_square + 1e-06) * section_gain[None]).astype(jnp.bfloat16)

def reference(embeddings, compress, mixing, rescale_factor, active_block_flags):
    outputs = []
    for section in range(RELAY_SECTIONS):
        outputs.append(one_section(embeddings[section], compress[section], mixing[section], rescale_factor[section], active_block_flags))
    stacked = jnp.stack(outputs)
    return jnp.roll(stacked, 1, axis=0)
```

```python
import math

import jax
import jax.numpy as jnp
from jax import lax
from jax.sharding import PartitionSpec as P


def shift(array, axis, by):
    count = lax.axis_size(axis)
    return lax.ppermute(array, axis, [(i, (i + by) % count) for i in range(count)])


def shards(embeddings, compress, mixing, rescale_factor, active_block_flags):
    own_panel = embeddings[0]
    device_rows, field_dev, feature_width = own_panel.shape
    owners = lax.axis_size("field")
    myself = lax.axis_index("field")
    compress_rows = compress[0]
    rank_size = compress_rows.shape[1]
    block_weights = lax.dynamic_slice_in_dim(compress_rows, myself * field_dev, field_dev, 0)
    reduced = jnp.einsum(
        "ak,rae->rke", block_weights, own_panel, preferred_element_type=jnp.float32
    ).astype(jnp.bfloat16)
    partners = jnp.concatenate(
        [shift(reduced, "field", 1), reduced, shift(reduced, "field", -1)], axis=1
    )
    products = jnp.einsum(
        "rae,rke->rak", own_panel, partners, preferred_element_type=jnp.float32
    ).reshape(device_rows, field_dev, 3, rank_size)
    block_activity = active_block_flags[0].astype(jnp.float32)
    pairwise_feature_product = jnp.einsum("rajk,j->rak", products, block_activity)
    rank_rows = (
        (pairwise_feature_product * (1.0 / math.sqrt(feature_width)))
        .astype(jnp.bfloat16)
        .reshape(device_rows, field_dev * rank_size)
    )
    pieces = lax.all_gather(rank_rows, "field", axis=0)
    pieces = lax.all_gather(pieces, "row", axis=0)
    weights = mixing[0]
    column_count = weights.shape[1]
    slabs = weights.reshape(owners, field_dev * rank_size, column_count)
    projected = jnp.einsum(
        "yfrc,fcd->yrd", pieces, slabs, preferred_element_type=jnp.float32
    )
    groups = pieces.shape[0]
    fields_each = field_dev // groups
    local_mix = projected.astype(jnp.bfloat16).reshape(
        groups * device_rows, fields_each, feature_width
    )
    mixed_back = lax.all_to_all(local_mix, "row", split_axis=0, concat_axis=1, tiled=True)
    summed = own_panel.astype(jnp.float32) + mixed_back.astype(jnp.float32)
    mean_square = jnp.mean(summed * summed, axis=-1, keepdims=True)
    normed = (summed * lax.rsqrt(mean_square + 1e-06) * rescale_factor[0][None]).astype(
        jnp.bfloat16
    )
    handed = shift(normed, "segment", 1)
    return handed[None]


def solution(mesh):
    placed = (
        P("segment", "row", "field", None),
        P("segment", None, None),
        P("segment", None, ("field", "row")),
        P("segment", "field", None),
        P("field", None),
    )
    return jax.shard_map(
        shards,
        mesh=mesh,
        in_specs=placed,
        out_specs=P("segment", "row", "field", None),
        check_vma=False,
    )
```

```python
import math

import jax
import jax.numpy as jnp
from jax import lax
from jax.sharding import PartitionSpec as P


def shift(array, axis, by):
    count = lax.axis_size(axis)
    return lax.ppermute(array, axis, [(i, (i + by) % count) for i in range(count)])


def shards(embeddings, compress, mixing, rescale_factor, active_block_flags):
    own_panel = embeddings[0]
    device_rows, field_dev, feature_width = own_panel.shape
    owners = lax.axis_size("field")
    myself = lax.axis_index("field")
    panel_before = shift(own_panel, "segment", 1)
    weights = shift(mixing[0], "segment", 1)
    gain = shift(rescale_factor[0], "segment", 1)
    compress_rows = compress[0]
    rank_size = compress_rows.shape[1]
    block_weights = lax.dynamic_slice_in_dim(compress_rows, myself * field_dev, field_dev, 0)
    reduced = jnp.einsum(
        "ak,rae->rke", block_weights, own_panel, preferred_element_type=jnp.float32
    ).astype(jnp.bfloat16)
    partners = jnp.concatenate(
        [shift(reduced, "field", 1), reduced, shift(reduced, "field", -1)], axis=1
    )
    products = jnp.einsum(
        "rae,rke->rak", own_panel, partners, preferred_element_type=jnp.float32
    ).reshape(device_rows, field_dev, 3, rank_size)
    block_activity = active_block_flags[0].astype(jnp.float32)
    pairwise_feature_product = jnp.einsum("rajk,j->rak", products, block_activity)
    rank_rows = (
        (pairwise_feature_product * (1.0 / math.sqrt(feature_width)))
        .astype(jnp.bfloat16)
        .reshape(device_rows, field_dev * rank_size)
    )
    rank_rows = shift(rank_rows, "segment", 1)
    pieces = lax.all_gather(rank_rows, "field", axis=0)
    pieces = lax.all_gather(pieces, "row", axis=0)
    column_count = weights.shape[1]
    slabs = weights.reshape(owners, field_dev * rank_size, column_count)
    projected = jnp.einsum(
        "yfrc,fcd->yrd", pieces, slabs, preferred_element_type=jnp.float32
    ).astype(jnp.bfloat16)
    groups = pieces.shape[0]
    fields_each = field_dev // groups
    gathered = lax.all_to_all(projected, "row", split_axis=0, concat_axis=0, tiled=True)
    mixed_back = (
        gathered.reshape(groups, device_rows, fields_each, feature_width)
        .transpose(1, 0, 2, 3)
        .reshape(device_rows, field_dev, feature_width)
    )
    summed = panel_before.astype(jnp.float32) + mixed_back.astype(jnp.float32)
    mean_square = jnp.mean(summed * summed, axis=-1, keepdims=True)
    normed = (summed * lax.rsqrt(mean_square + 1e-06) * gain[None]).astype(jnp.bfloat16)
    return normed[None]


def solution(mesh):
    placed = (
        P("segment", "row", "field", None),
        P("segment", None, None),
        P("segment", None, ("field", "row")),
        P("segment", "field", None),
        P("field", None),
    )
    return jax.shard_map(
        shards,
        mesh=mesh,
        in_specs=placed,
        out_specs=P("segment", "row", "field", None),
        check_vma=False,
    )
```

```python
import math

import jax
import jax.numpy as jnp
from jax import lax
from jax.sharding import PartitionSpec as P


def shift(array, axis, by):
    count = lax.axis_size(axis)
    return lax.ppermute(array, axis, [(i, (i + by) % count) for i in range(count)])


def shards(embeddings, compress, mixing, rescale_factor, active_block_flags):
    own_panel = embeddings[0]
    device_rows, field_dev, feature_width = own_panel.shape
    groups = lax.axis_size("row")
    myself = lax.axis_index("field")
    fields_each = field_dev // groups
    panel_before = shift(own_panel, "segment", 1)
    weights = shift(mixing[0], "segment", 1)
    gain = shift(rescale_factor[0], "segment", 1)
    panel_t = (
        panel_before.reshape(device_rows, groups, fields_each, feature_width)
        .transpose(1, 2, 0, 3)
        .astype(jnp.float32)
    )
    gain_t = gain.reshape(groups, fields_each, 1, feature_width)
    compress_rows = compress[0]
    rank_size = compress_rows.shape[1]
    block_weights = lax.dynamic_slice_in_dim(compress_rows, myself * field_dev, field_dev, 0)
    reduced = jnp.einsum(
        "ak,rae->rke", block_weights, own_panel, preferred_element_type=jnp.float32
    ).astype(jnp.bfloat16)
    partners = jnp.concatenate(
        [shift(reduced, "field", 1), reduced, shift(reduced, "field", -1)], axis=1
    )
    products = jnp.einsum(
        "rae,rke->rak", own_panel, partners, preferred_element_type=jnp.float32
    ).reshape(device_rows, field_dev, 3, rank_size)
    block_activity = active_block_flags[0].astype(jnp.float32)
    pairwise_feature_product = jnp.einsum("rajk,j->rak", products, block_activity)
    rank_rows = (
        (pairwise_feature_product * (1.0 / math.sqrt(feature_width)))
        .astype(jnp.bfloat16)
        .reshape(device_rows, field_dev * rank_size)
    )
    rank_rows = shift(rank_rows, "segment", 1)
    flat = lax.all_gather(rank_rows, "field", axis=1, tiled=True)
    flat = lax.all_gather(flat, "row", axis=0, tiled=True)
    projected = jnp.einsum(
        "rk,kfe->fre",
        flat,
        weights.reshape(-1, fields_each, feature_width),
        preferred_element_type=jnp.float32,
    ).astype(jnp.bfloat16)
    projected = projected.reshape(fields_each, groups, device_rows, feature_width).transpose(1, 0, 2, 3)
    gathered = lax.all_to_all(projected, "row", split_axis=0, concat_axis=0, tiled=True)
    summed = panel_t + gathered.astype(jnp.float32)
    mean_square = jnp.mean(summed * summed, axis=-1, keepdims=True)
    normed = (summed * lax.rsqrt(mean_square + 1e-06) * gain_t).astype(jnp.bfloat16)
    normed = normed.transpose(2, 0, 1, 3).reshape(device_rows, field_dev, feature_width)
    return normed[None]


def solution(mesh):
    placed = (
        P("segment", "row", "field", None),
        P("segment", None, None),
        P("segment", None, ("field", "row")),
        P("segment", "field", None),
        P("field", None),
    )
    return jax.shard_map(
        shards,
        mesh=mesh,
        in_specs=placed,
        out_specs=P("segment", "row", "field", None),
        check_vma=False,
    )
```

```python
import math

import jax
import jax.numpy as jnp
from jax import lax
from jax.sharding import PartitionSpec as P


def shift(array, axis, by):
    count = lax.axis_size(axis)
    return lax.ppermute(array, axis, [(i, (i + by) % count) for i in range(count)])


def shards(embeddings, compress, mixing, rescale_factor, active_block_flags):
    own_panel = embeddings[0]
    device_rows, field_dev, feature_width = own_panel.shape
    groups = lax.axis_size("row")
    myself = lax.axis_index("field")
    fields_each = field_dev // groups
    panel_before = shift(own_panel, "segment", 1)
    weights = shift(mixing[0], "segment", 1)
    gain = shift(rescale_factor[0], "segment", 1)
    panel_t = (
        panel_before.reshape(device_rows, groups, fields_each, feature_width)
        .transpose(1, 2, 0, 3)
        .astype(jnp.float32)
    )
    gain_t = gain.reshape(groups, fields_each, 1, feature_width)
    compress_rows = compress[0]
    rank_size = compress_rows.shape[1]
    block_weights = lax.dynamic_slice_in_dim(compress_rows, myself * field_dev, field_dev, 0)
    reduced = jnp.einsum(
        "ak,rae->rke", block_weights, own_panel, preferred_element_type=jnp.float32
    ).astype(jnp.bfloat16)
    partners = jnp.concatenate(
        [shift(reduced, "field", 1), reduced, shift(reduced, "field", -1)], axis=1
    )
    products = jnp.einsum(
        "rae,rke->rak", own_panel, partners, preferred_element_type=jnp.float32
    ).reshape(device_rows, field_dev, 3, rank_size)
    block_activity = active_block_flags[0].astype(jnp.float32)
    pairwise_feature_product = jnp.einsum("rajk,j->rak", products, block_activity)
    rank_rows = (
        (pairwise_feature_product * (1.0 / math.sqrt(feature_width)))
        .astype(jnp.bfloat16)
        .reshape(device_rows, field_dev * rank_size)
    )
    rank_rows = shift(rank_rows, "segment", 1)
    flat = lax.all_gather(rank_rows, "field", axis=1, tiled=True)
    columns = weights.reshape(-1, fields_each, feature_width)

    def project(block):
        return jnp.einsum(
            "rk,kfe->fre", block, columns, preferred_element_type=jnp.float32
        ).astype(jnp.bfloat16)

    relative = [None] * groups
    relative[0] = project(flat)
    ahead, behind = flat, flat
    for step in range(1, groups // 2 + 1):
        ahead = shift(ahead, "row", 1)
        relative[step] = shift(project(ahead), "row", -step)
        if step < groups - step:
            behind = shift(behind, "row", -1)
            relative[groups - step] = shift(project(behind), "row", step)
    stacked = jnp.stack(relative)
    doubled = jnp.concatenate([stacked, stacked], axis=0)
    place = lax.axis_index("row")
    gathered = lax.dynamic_slice_in_dim(doubled, groups - place, groups, 0)
    summed = panel_t + gathered.astype(jnp.float32)
    mean_square = jnp.mean(summed * summed, axis=-1, keepdims=True)
    normed = (summed * lax.rsqrt(mean_square + 1e-06) * gain_t).astype(jnp.bfloat16)
    normed = normed.transpose(2, 0, 1, 3).reshape(device_rows, field_dev, feature_width)
    return normed[None]


def solution(mesh):
    placed = (
        P("segment", "row", "field", None),
        P("segment", None, None),
        P("segment", None, ("field", "row")),
        P("segment", "field", None),
        P("field", None),
    )
    return jax.shard_map(
        shards,
        mesh=mesh,
        in_specs=placed,
        out_specs=P("segment", "row", "field", None),
        check_vma=False,
    )
```

```python
import math

import jax
import jax.numpy as jnp
from jax import lax
from jax.sharding import PartitionSpec as P


def shift(array, axis, by):
    count = lax.axis_size(axis)
    return lax.ppermute(array, axis, [(i, (i + by) % count) for i in range(count)])


def shards(embeddings, compress, mixing, rescale_factor, active_block_flags):
    own_panel = embeddings[0]
    device_rows, field_dev, feature_width = own_panel.shape
    groups = lax.axis_size("row")
    myself = lax.axis_index("field")
    fields_each = field_dev // groups
    weights = shift(mixing[0], "segment", 1)
    compress_rows = compress[0]
    rank_size = compress_rows.shape[1]
    block_weights = lax.dynamic_slice_in_dim(compress_rows, myself * field_dev, field_dev, 0)
    reduced = jnp.einsum(
        "ak,rae->rke", block_weights, own_panel, preferred_element_type=jnp.float32
    ).astype(jnp.bfloat16)
    partners = jnp.concatenate(
        [shift(reduced, "field", 1), reduced, shift(reduced, "field", -1)], axis=1
    )
    products = jnp.einsum(
        "rae,rke->rak", own_panel, partners, preferred_element_type=jnp.float32
    ).reshape(device_rows, field_dev, 3, rank_size)
    block_activity = active_block_flags[0].astype(jnp.float32)
    pairwise_feature_product = jnp.einsum("rajk,j->rak", products, block_activity)
    rank_rows = (
        (pairwise_feature_product * (1.0 / math.sqrt(feature_width)))
        .astype(jnp.bfloat16)
        .reshape(device_rows, field_dev * rank_size)
    )
    weights, rank_rows = lax.optimization_barrier((weights, rank_rows))
    rank_rows = shift(rank_rows, "segment", 1)
    later, rank_rows = lax.optimization_barrier(((own_panel, rescale_factor[0]), rank_rows))
    panel_before = shift(later[0], "segment", 1)
    gain = shift(later[1], "segment", 1)
    panel_t = (
        panel_before.reshape(device_rows, groups, fields_each, feature_width)
        .transpose(1, 2, 0, 3)
        .astype(jnp.float32)
    )
    gain_t = gain.reshape(groups, fields_each, 1, feature_width)
    flat = lax.all_gather(rank_rows, "field", axis=1, tiled=True)
    columns = weights.reshape(-1, fields_each, feature_width)

    def project(block):
        return jnp.einsum(
            "rk,kfe->fre", block, columns, preferred_element_type=jnp.float32
        ).astype(jnp.bfloat16)

    relative = [None] * groups
    relative[0] = project(flat)
    ahead, behind = flat, flat
    for step in range(1, groups // 2 + 1):
        ahead = shift(ahead, "row", 1)
        relative[step] = shift(project(ahead), "row", -step)
        if step < groups - step:
            behind = shift(behind, "row", -1)
            relative[groups - step] = shift(project(behind), "row", step)
    stacked = jnp.stack(relative)
    doubled = jnp.concatenate([stacked, stacked], axis=0)
    place = lax.axis_index("row")
    gathered = lax.dynamic_slice_in_dim(doubled, groups - place, groups, 0)
    summed = panel_t + gathered.astype(jnp.float32)
    mean_square = jnp.mean(summed * summed, axis=-1, keepdims=True)
    normed = (summed * lax.rsqrt(mean_square + 1e-06) * gain_t).astype(jnp.bfloat16)
    normed = normed.transpose(2, 0, 1, 3).reshape(device_rows, field_dev, feature_width)
    return normed[None]


def solution(mesh):
    placed = (
        P("segment", "row", "field", None),
        P("segment", None, None),
        P("segment", None, ("field", "row")),
        P("segment", "field", None),
        P("field", None),
    )
    return jax.shard_map(
        shards,
        mesh=mesh,
        in_specs=placed,
        out_specs=P("segment", "row", "field", None),
        check_vma=False,
    )
```

```python
import math

import jax
import jax.numpy as jnp
from jax import lax
from jax.sharding import PartitionSpec as P


def shift(array, axis, by):
    count = lax.axis_size(axis)
    return lax.ppermute(array, axis, [(i, (i + by) % count) for i in range(count)])


def shards(embeddings, compress, mixing, rescale_factor, active_block_flags):
    own_panel = embeddings[0]
    device_rows, field_dev, feature_width = own_panel.shape
    groups = lax.axis_size("row")
    myself = lax.axis_index("field")
    fields_each = field_dev // groups
    weights = shift(mixing[0], "segment", 1)
    compress_rows = compress[0]
    rank_size = compress_rows.shape[1]
    block_weights = lax.dynamic_slice_in_dim(compress_rows, myself * field_dev, field_dev, 0)
    reduced = jnp.einsum(
        "ak,rae->rke", block_weights, own_panel, preferred_element_type=jnp.float32
    ).astype(jnp.bfloat16)
    partners = jnp.concatenate(
        [shift(reduced, "field", 1), reduced, shift(reduced, "field", -1)], axis=1
    )
    products = jnp.einsum(
        "rae,rke->rak", own_panel, partners, preferred_element_type=jnp.float32
    ).reshape(device_rows, field_dev, 3, rank_size)
    block_activity = active_block_flags[0].astype(jnp.float32)
    pairwise_feature_product = jnp.einsum("rajk,j->rak", products, block_activity)
    rank_rows = (
        (pairwise_feature_product * (1.0 / math.sqrt(feature_width)))
        .astype(jnp.bfloat16)
        .reshape(device_rows, field_dev * rank_size)
    )
    weights, rank_rows = lax.optimization_barrier((weights, rank_rows))
    rank_rows = shift(rank_rows, "segment", 1)
    later, rank_rows = lax.optimization_barrier(((own_panel, rescale_factor[0]), rank_rows))
    panel_before = shift(later[0], "segment", 1)
    gain = shift(later[1], "segment", 1)
    panel_t = (
        panel_before.reshape(device_rows, groups, fields_each, feature_width)
        .transpose(1, 2, 0, 3)
        .astype(jnp.float32)
    )
    gain_t = gain.reshape(groups, fields_each, 1, feature_width)
    flat = lax.all_gather(rank_rows, "field", axis=1, tiled=True)
    columns = weights.reshape(-1, fields_each, feature_width)

    def project(block):
        return jnp.einsum(
            "rk,kfe->fre", block, columns, preferred_element_type=jnp.float32
        ).astype(jnp.bfloat16)

    relative = [None] * groups
    relative[0] = project(flat)
    ahead, behind = flat, flat
    for step in range(1, groups // 2 + 1):
        ahead = shift(ahead, "row", 1)
        relative[step] = shift(project(ahead), "row", -step)
        if step < groups - step:
            behind = shift(behind, "row", -1)
            relative[groups - step] = shift(project(behind), "row", step)
    stacked = jnp.stack(relative)
    place = lax.axis_index("row")
    order = (jnp.arange(groups, dtype=jnp.int32) - place) % groups
    gathered = jnp.take(stacked, order, axis=0)
    summed = panel_t + gathered.astype(jnp.float32)
    mean_square = jnp.mean(summed * summed, axis=-1, keepdims=True)
    normed = (summed * lax.rsqrt(mean_square + 1e-06) * gain_t).astype(jnp.bfloat16)
    normed = normed.transpose(2, 0, 1, 3).reshape(device_rows, field_dev, feature_width)
    return normed[None]


def solution(mesh):
    placed = (
        P("segment", "row", "field", None),
        P("segment", None, None),
        P("segment", None, ("field", "row")),
        P("segment", "field", None),
        P("field", None),
    )
    return jax.shard_map(
        shards,
        mesh=mesh,
        in_specs=placed,
        out_specs=P("segment", "row", "field", None),
        check_vma=False,
    )
```

```python
import math

import jax
import jax.numpy as jnp
from jax import lax
from jax.sharding import PartitionSpec as P


def shift(array, axis, by):
    count = lax.axis_size(axis)
    return lax.ppermute(array, axis, [(i, (i + by) % count) for i in range(count)])


def onward(array, by):
    sections = lax.axis_size("segment")
    count = lax.axis_size("row")
    pairs = [
        (seg * count + i, ((seg + 1) % sections) * count + (i + by) % count)
        for seg in range(sections)
        for i in range(count)
    ]
    return lax.ppermute(array, ("segment", "row"), pairs)


def shards(embeddings, compress, mixing, rescale_factor, active_block_flags):
    own_panel = embeddings[0]
    device_rows, field_dev, feature_width = own_panel.shape
    groups = lax.axis_size("row")
    myself = lax.axis_index("field")
    fields_each = field_dev // groups
    weights = mixing[0]
    panel_before = shift(own_panel, "segment", 1)
    gain = shift(rescale_factor[0], "segment", 1)
    compress_rows = compress[0]
    rank_size = compress_rows.shape[1]
    block_weights = lax.dynamic_slice_in_dim(compress_rows, myself * field_dev, field_dev, 0)
    reduced = jnp.einsum(
        "ak,rae->rke", block_weights, own_panel, preferred_element_type=jnp.float32
    ).astype(jnp.bfloat16)
    partners = jnp.concatenate(
        [shift(reduced, "field", 1), reduced, shift(reduced, "field", -1)], axis=1
    )
    products = jnp.einsum(
        "rae,rke->rak", own_panel, partners, preferred_element_type=jnp.float32
    ).reshape(device_rows, field_dev, 3, rank_size)
    block_activity = active_block_flags[0].astype(jnp.float32)
    pairwise_feature_product = jnp.einsum("rajk,j->rak", products, block_activity)
    rank_rows = (
        (pairwise_feature_product * (1.0 / math.sqrt(feature_width)))
        .astype(jnp.bfloat16)
        .reshape(device_rows, field_dev * rank_size)
    )
    panel_t = (
        panel_before.reshape(device_rows, groups, fields_each, feature_width)
        .transpose(1, 2, 0, 3)
        .astype(jnp.float32)
    )
    gain_t = gain.reshape(groups, fields_each, 1, feature_width)
    flat = lax.all_gather(rank_rows, "field", axis=1, tiled=True)
    columns = weights.reshape(-1, fields_each, feature_width)

    def project(block):
        return jnp.einsum(
            "rk,kfe->fre", block, columns, preferred_element_type=jnp.float32
        ).astype(jnp.bfloat16)

    relative = [None] * groups
    relative[0] = onward(project(flat), 0)
    ahead, behind = flat, flat
    for step in range(1, groups // 2 + 1):
        ahead = shift(ahead, "row", 1)
        relative[step] = onward(project(ahead), -step)
        if step < groups - step:
            behind = shift(behind, "row", -1)
            relative[groups - step] = onward(project(behind), step)
    stacked = jnp.stack(relative)
    place = lax.axis_index("row")
    order = (jnp.arange(groups, dtype=jnp.int32) - place) % groups
    gathered = jnp.take(stacked, order, axis=0)
    summed = panel_t + gathered.astype(jnp.float32)
    mean_square = jnp.mean(summed * summed, axis=-1, keepdims=True)
    normed = (summed * lax.rsqrt(mean_square + 1e-06) * gain_t).astype(jnp.bfloat16)
    normed = normed.transpose(2, 0, 1, 3).reshape(device_rows, field_dev, feature_width)
    return normed[None]


def solution(mesh):
    placed = (
        P("segment", "row", "field", None),
        P("segment", None, None),
        P("segment", None, ("field", "row")),
        P("segment", "field", None),
        P("field", None),
    )
    return jax.shard_map(
        shards,
        mesh=mesh,
        in_specs=placed,
        out_specs=P("segment", "row", "field", None),
        check_vma=False,
    )
```

```python
import math

import jax
import jax.numpy as jnp
from jax import lax
from jax.sharding import PartitionSpec as P


def shift(array, axis, by):
    count = lax.axis_size(axis)
    return lax.ppermute(array, axis, [(i, (i + by) % count) for i in range(count)])


def onward(array, by):
    sections = lax.axis_size("segment")
    count = lax.axis_size("row")
    pairs = [
        (seg * count + i, ((seg + 1) % sections) * count + (i + by) % count)
        for seg in range(sections)
        for i in range(count)
    ]
    return lax.ppermute(array, ("segment", "row"), pairs)


def shards(embeddings, compress, mixing, rescale_factor, active_block_flags):
    own_panel = embeddings[0]
    device_rows, field_dev, feature_width = own_panel.shape
    groups = lax.axis_size("row")
    myself = lax.axis_index("field")
    fields_each = field_dev // groups
    weights = mixing[0]
    panel_before = shift(own_panel, "segment", 1)
    gain = shift(rescale_factor[0], "segment", 1)
    compress_rows = compress[0]
    rank_size = compress_rows.shape[1]
    block_weights = lax.dynamic_slice_in_dim(compress_rows, myself * field_dev, field_dev, 0)
    reduced = jnp.einsum(
        "ak,rae->rke", block_weights, own_panel, preferred_element_type=jnp.float32
    ).astype(jnp.bfloat16)
    partners = jnp.concatenate(
        [shift(reduced, "field", 1), reduced, shift(reduced, "field", -1)], axis=1
    )
    products = jnp.einsum(
        "rae,rke->rak", own_panel, partners, preferred_element_type=jnp.float32
    ).reshape(device_rows, field_dev, 3, rank_size)
    block_activity = active_block_flags[0].astype(jnp.float32)
    pairwise_feature_product = jnp.einsum("rajk,j->rak", products, block_activity)
    rank_rows = (
        (pairwise_feature_product * (1.0 / math.sqrt(feature_width)))
        .astype(jnp.bfloat16)
        .reshape(device_rows, field_dev * rank_size)
    )
    panel_t = (
        panel_before.reshape(device_rows, groups, fields_each, feature_width)
        .transpose(1, 2, 0, 3)
        .astype(jnp.float32)
    )
    gain_t = gain.reshape(groups, fields_each, 1, feature_width)
    flat = lax.all_gather(rank_rows, "field", axis=1, tiled=True)
    columns = weights.reshape(-1, fields_each, feature_width)

    def project(block):
        return jnp.einsum(
            "rk,kfe->fre", block, columns, preferred_element_type=jnp.float32
        ).astype(jnp.bfloat16)

    place = lax.axis_index("row")
    arrival = (jnp.arange(groups, dtype=jnp.int32) + place) % groups
    panel_r = jnp.take(panel_t, arrival, axis=0, mode="clip")
    gain_r = jnp.take(gain_t, arrival, axis=0, mode="clip")

    def finish(block, offset):
        summed = panel_r[offset] + block.astype(jnp.float32)
        mean_square = jnp.mean(summed * summed, axis=-1, keepdims=True)
        return (summed * lax.rsqrt(mean_square + 1e-06) * gain_r[offset]).astype(jnp.bfloat16)

    relative = [None] * groups
    relative[0] = finish(onward(project(flat), 0), 0)
    ahead, behind = flat, flat
    for step in range(1, groups // 2 + 1):
        ahead = shift(ahead, "row", 1)
        relative[step] = finish(onward(project(ahead), -step), step)
        if step < groups - step:
            behind = shift(behind, "row", -1)
            relative[groups - step] = finish(onward(project(behind), step), groups - step)
    stacked = jnp.stack(relative)
    order = (jnp.arange(groups, dtype=jnp.int32) - place) % groups
    normed = jnp.take(stacked, order, axis=0, mode="clip")
    normed = normed.transpose(2, 0, 1, 3).reshape(device_rows, field_dev, feature_width)
    return normed[None]


def solution(mesh):
    placed = (
        P("segment", "row", "field", None),
        P("segment", None, None),
        P("segment", None, ("field", "row")),
        P("segment", "field", None),
        P("field", None),
    )
    return jax.shard_map(
        shards,
        mesh=mesh,
        in_specs=placed,
        out_specs=P("segment", "row", "field", None),
        check_vma=False,
    )
```
